128 devices in a mesh: band: 32 (over z, y, x_hi), slab: 4 (over x_lo, core).
Axes of the slice: x: 4 (x_hi: 2, x_lo: 2; x = x_hi * 2 + x_lo), y: 4, z: 4, core: 2. Of those that a mesh axis runs over, the one named last changes fastest.
Arguments:
- coeffs: float32 [128, 2, 48, 2304], P(('band', 'slab')), may hold values from -6 to 6
- occupation: float32 [128], P(('band', 'slab')), may hold values from 0.5 to 2
- core_density: float32 [96, 96, 96], replicated, may hold values from 0.2 to 5
- external: float32 [96, 96, 96], replicated, may hold values from -4 to 4
Outputs:
- new_coeffs: float32 [128, 2, 48, 2304], P(('band', 'slab'))
- potential: float32 [96, 96, 96], replicated
- energy: float32 [], replicated
The draws below stay inside these ranges and needn't reach their ends.
All inputs are finite; a program needn't handle non-finite values.
Results may differ from the reference program's by a relative error of at most 0.0003.
Values sent between devices are 32-bit elements; how exact they have to be, the bound alone decides.
No kernel may reach another device: no remote copies, remote signals or barrier semaphores. Data moves between devices by JAX's collectives and lax.ppermute only.
A program may use at most 128 MiB of HBM per device.

```python
import math
import jax
import jax.numpy as jnp
from jax import lax

GC = 48
NG = 96
BANDS = 128


def shard_levels(stream_key, extent, cuts, least, high):
    def one(dim, parts):
        heights = jax.random.uniform(jax.random.fold_in(jax.random.fold_in(stream_key, 6), dim), (parts,), jnp.float32, least / len(cuts), high / len(cuts))
        return jnp.repeat(jnp.exp(heights), extent[dim] // parts).reshape((-1,) + (1,) * (len(extent) - dim - 1))

    factor_of = one(*cuts[0])
    for cut in cuts[1:]:
        factor_of = factor_of * one(*cut)
    return factor_of


def noise(own_key, extent, scale, limit, split=(), held_as=jnp.bfloat16):
    gain = shard_levels(own_key, extent, split, -0.22, 0.18) if split else 1.0
    drawn = jax.random.normal(own_key, extent, jnp.float32) * scale * gain
    return jnp.minimum(jnp.maximum(drawn, -limit), limit).astype(held_as)


def setup_inputs(seed: int = 0) -> dict:
    splits = jax.random.split(jax.random.key(seed), 5)
    return {
        "coeffs": noise(splits[0], (BANDS, 2, GC, GC * GC), 1.0, 6.0, ((0, 128),), jnp.float32),
        "occupation": jnp.clip(0.5 + 1.5 * jax.random.uniform(splits[1], (BANDS,), jnp.float32) ** shard_levels(splits[1], (BANDS,), ((0, 128),), -0.2, 0.2), 0.5, 2.0),
        "core_density": jnp.clip(jnp.exp(jax.random.uniform(splits[2], (NG, NG, NG), jnp.float32, math.log(0.2), math.log(5.0))), 0.2, 5.0),
        "external": noise(splits[3], (NG, NG, NG), 1.0, 4.0, (), jnp.float32),
    }


TWO_PI = 2.0 * math.pi
FOUR_PI = 4.0 * math.pi
SCREEN = 0.05
STEP_DT = 0.1
XC_COEF = -((3.0 / math.pi) ** (1.0 / 3.0))


def contract(operand, table, position):
    labels = "abcd"[:operand.ndim]
    pattern = labels + ",r" + labels[position] + "->" + labels[:position] + "r" + labels[position + 1:]
    return jnp.einsum(pattern, operand, table, precision=lax.Precision.HIGHEST)


def transform_axis(real_in, imag_in, tables, position):
    cosine, sine = tables
    real_out = contract(real_in, cosine, position) - contract(imag_in, sine, position)
    imag_out = contract(real_in, sine, position) + contract(imag_in, cosine, position)
    return real_out, imag_out


def real_input_axis(values, tables, position):
    return contract(values, tables[0], position), contract(values, tables[1], position)


def real_output_axis(real_in, imag_in, tables, position):
    return contract(real_in, tables[0], position) - contract(imag_in, tables[1], position)


def phase_table(outer, inner, sign_value, factor):
    product = jnp.mod(outer[:, None] * inner[None, :], NG)
    angles = (sign_value * TWO_PI / NG) * product.astype(jnp.float32)
    return jnp.cos(angles) * factor, jnp.sin(angles) * factor


def frequencies():
    return jnp.arange(GC, dtype=jnp.int32) - GC // 2


def wave_tables():
    points = jnp.arange(NG, dtype=jnp.int32)
    return phase_table(points, frequencies(), 1.0, 1.0), phase_table(frequencies(), points, -1.0, 1.0 / NG)


def poisson_tables():
    points = jnp.arange(NG, dtype=jnp.int32)
    return phase_table(points, points, -1.0, 1.0 / NG), phase_table(points, points, 1.0, 1.0)


def kinetic_table():
    squares = (frequencies().astype(jnp.float32) * (TWO_PI / NG)) ** 2
    return 0.5 * (squares[:, None, None] + squares[None, :, None] + squares[None, None, :])


def folded_squares(start, count):
    index = start + jnp.arange(count, dtype=jnp.int32)
    folded = jnp.where(index < NG // 2, index, index - NG)
    return (folded.astype(jnp.float32) * (TWO_PI / NG)) ** 2, folded == 0


def screened_kernel(start_x, count_x, start_y, count_y, start_z, count_z):
    square_x, zero_x = folded_squares(start_x, count_x)
    square_y, zero_y = folded_squares(start_y, count_y)
    square_z, zero_z = folded_squares(start_z, count_z)
    total = square_x[:, None, None] + square_y[None, :, None] + square_z[None, None, :]
    anchor = zero_x[:, None, None] & zero_y[None, :, None] & zero_z[None, None, :]
    return jnp.where(anchor, 0.0, FOUR_PI / (total + SCREEN))


def to_grid(real_in, imag_in, forward, offset):
    for position in (offset + 2, offset + 1, offset):
        real_in, imag_in = transform_axis(real_in, imag_in, forward, position)
    return real_in, imag_in


def to_coeffs(real_in, imag_in, backward, offset):
    for position in (offset, offset + 1, offset + 2):
        real_in, imag_in = transform_axis(real_in, imag_in, backward, position)
    return real_in, imag_in


def propagate(real_in, imag_in, grid_r, grid_i, potential, kinetic, forward, backward, offset):
    back_r, back_i = to_coeffs(potential * grid_r, potential * grid_i, backward, offset)
    first_r = kinetic * real_in + back_r
    first_i = kinetic * imag_in + back_i
    next_r, next_i = to_grid(first_r, first_i, forward, offset)
    back_r, back_i = to_coeffs(potential * next_r, potential * next_i, backward, offset)
    second_r = kinetic * first_r + back_r
    second_i = kinetic * first_i + back_i
    new_r = real_in + STEP_DT * first_i - 0.5 * STEP_DT * STEP_DT * second_r
    new_i = imag_in - STEP_DT * first_r - 0.5 * STEP_DT * STEP_DT * second_i
    return new_r, new_i, first_r, first_i


def poisson_full(density):
    forward, inverse = poisson_tables()
    real_part, imag_part = real_input_axis(density, forward, 2)
    real_part, imag_part = transform_axis(real_part, imag_part, forward, 1)
    real_part, imag_part = transform_axis(real_part, imag_part, forward, 0)
    kernel = screened_kernel(0, NG, 0, NG, 0, NG)
    real_part, imag_part = real_part * kernel, imag_part * kernel
    real_part, imag_part = transform_axis(real_part, imag_part, inverse, 0)
    real_part, imag_part = transform_axis(real_part, imag_part, inverse, 1)
    return real_output_axis(real_part, imag_part, inverse, 2)


def reference(coeffs, occupation, core_density, external):
    forward, backward = wave_tables()
    kinetic = kinetic_table()
    total_bands = coeffs.shape[0]
    waves = coeffs.reshape(total_bands, 2, GC, GC, GC)
    weights = occupation / (GC * GC * GC * total_bands)

    def accumulate(density, item):
        wave, weight = item
        grid_r, grid_i = to_grid(wave[0], wave[1], forward, 0)
        return density + weight * (grid_r * grid_r + grid_i * grid_i), weight

    scanned = lax.scan(accumulate, jnp.zeros((NG, NG, NG), jnp.float32), (waves, weights))
    density = scanned[0]
    potential = external + poisson_full(density) + XC_COEF * jnp.cbrt(density + core_density)

    def advance(item):
        wave, weight = item
        grid_r, grid_i = to_grid(wave[0], wave[1], forward, 0)
        new_r, new_i, first_r, first_i = propagate(wave[0], wave[1], grid_r, grid_i, potential, kinetic, forward, backward, 0)
        band_value = weight * jnp.sum(wave[0] * first_r + wave[1] * first_i)
        return jnp.stack([new_r, new_i]).reshape(2, GC, GC * GC), band_value

    new_waves, energies = lax.map(advance, (waves, weights))
    return new_waves, potential, jnp.sum(energies)
```

```python
import math

import jax
import jax.numpy as jnp
from jax import lax
from jax.sharding import PartitionSpec as P

GC = 48
NG = 96


TWO_PI = 2.0 * math.pi
FOUR_PI = 4.0 * math.pi
SCREEN = 0.05
STEP_DT = 0.1
XC_COEF = -((3.0 / math.pi) ** (1.0 / 3.0))


def contract(operand, table, position):
    labels = "abcd"[: operand.ndim]
    pattern = (
        labels + ",r" + labels[position] + "->" + labels[:position] + "r" + labels[position + 1 :]
    )
    return jnp.einsum(pattern, operand, table, precision=lax.Precision.HIGHEST)


def transform_axis(real_in, imag_in, tables, position):
    cosine, sine = tables
    real_out = contract(real_in, cosine, position) - contract(imag_in, sine, position)
    imag_out = contract(real_in, sine, position) + contract(imag_in, cosine, position)
    return (real_out, imag_out)


def real_input_axis(values, tables, position):
    return (contract(values, tables[0], position), contract(values, tables[1], position))


def real_output_axis(real_in, imag_in, tables, position):
    return contract(real_in, tables[0], position) - contract(imag_in, tables[1], position)


def phase_table(outer, inner, sign_value, factor):
    product = jnp.mod(outer[:, None] * inner[None, :], NG)
    angles = sign_value * TWO_PI / NG * product.astype(jnp.float32)
    return (jnp.cos(angles) * factor, jnp.sin(angles) * factor)


def frequencies():
    return jnp.arange(GC, dtype=jnp.int32) - GC // 2


def wave_tables():
    points = jnp.arange(NG, dtype=jnp.int32)
    return (
        phase_table(points, frequencies(), 1.0, 1.0),
        phase_table(frequencies(), points, -1.0, 1.0 / NG),
    )


def poisson_tables():
    points = jnp.arange(NG, dtype=jnp.int32)
    return (phase_table(points, points, -1.0, 1.0 / NG), phase_table(points, points, 1.0, 1.0))


def kinetic_table():
    squares = (frequencies().astype(jnp.float32) * (TWO_PI / NG)) ** 2
    return 0.5 * (squares[:, None, None] + squares[None, :, None] + squares[None, None, :])


def folded_squares(start, count):
    index = start + jnp.arange(count, dtype=jnp.int32)
    folded = jnp.where(index < NG // 2, index, index - NG)
    return ((folded.astype(jnp.float32) * (TWO_PI / NG)) ** 2, folded == 0)


def screened_kernel(start_x, count_x, start_y, count_y, start_z, count_z):
    square_x, zero_x = folded_squares(start_x, count_x)
    square_y, zero_y = folded_squares(start_y, count_y)
    square_z, zero_z = folded_squares(start_z, count_z)
    total = square_x[:, None, None] + square_y[None, :, None] + square_z[None, None, :]
    anchor = zero_x[:, None, None] & zero_y[None, :, None] & zero_z[None, None, :]
    return jnp.where(anchor, 0.0, FOUR_PI / (total + SCREEN))


def to_grid(real_in, imag_in, forward, offset):
    for position in (offset + 2, offset + 1, offset):
        real_in, imag_in = transform_axis(real_in, imag_in, forward, position)
    return (real_in, imag_in)


def to_coeffs(real_in, imag_in, backward, offset):
    for position in (offset, offset + 1, offset + 2):
        real_in, imag_in = transform_axis(real_in, imag_in, backward, position)
    return (real_in, imag_in)


def propagate(real_in, imag_in, grid_r, grid_i, potential, kinetic, forward, backward, offset):
    back_r, back_i = to_coeffs(potential * grid_r, potential * grid_i, backward, offset)
    first_r = kinetic * real_in + back_r
    first_i = kinetic * imag_in + back_i
    next_r, next_i = to_grid(first_r, first_i, forward, offset)
    back_r, back_i = to_coeffs(potential * next_r, potential * next_i, backward, offset)
    second_r = kinetic * first_r + back_r
    second_i = kinetic * first_i + back_i
    new_r = real_in + STEP_DT * first_i - 0.5 * STEP_DT * STEP_DT * second_r
    new_i = imag_in - STEP_DT * first_r - 0.5 * STEP_DT * STEP_DT * second_i
    return (new_r, new_i, first_r, first_i)


def local_terms(density_part, core_part, external_part, hartree_part):
    return external_part + hartree_part + XC_COEF * jnp.cbrt(density_part + core_part)


def reduce_density(partial_value, kinetic_part):
    band_count = lax.axis_size("band")
    slab_count = lax.axis_size("slab")
    rows_x = NG // band_count
    rows_y = NG // slab_count
    pieces = partial_value.reshape(band_count, rows_x, slab_count, rows_y, NG)
    pieces = pieces.transpose(0, 2, 1, 3, 4).reshape(band_count * slab_count, rows_x, rows_y, NG)
    extra = jnp.zeros(pieces.shape[:-1] + (1,), jnp.float32).at[:, 0, 0, 0].set(kinetic_part)
    pieces = jnp.concatenate([pieces, extra], axis=-1)
    pieces = lax.all_to_all(pieces, ("band", "slab"), 0, 0, tiled=True)
    block = jnp.sum(pieces, axis=0)
    kinetic_total = block[0, 0, NG]
    block = block[..., :NG]
    spread = jnp.broadcast_to(block[None], (band_count,) + block.shape)
    spread = lax.all_to_all(spread, "band", 0, 0, tiled=True)
    return spread.reshape(NG, rows_y, NG), kinetic_total


def slab_potential(partial_value, kinetic_part, core_density, external):
    slab_count = lax.axis_size("slab")
    rows = NG // slab_count
    slab_place = lax.axis_index("slab")
    forward, inverse = poisson_tables()
    share, kinetic_total = reduce_density(partial_value, kinetic_part)
    real_part, imag_part = real_input_axis(share, forward, 2)
    real_part, imag_part = transform_axis(real_part, imag_part, forward, 0)
    both = lax.all_to_all(jnp.stack([real_part, imag_part]), "slab", 1, 2, tiled=True)
    real_part, imag_part = both[0], both[1]
    real_part, imag_part = transform_axis(real_part, imag_part, forward, 1)
    kernel = screened_kernel(slab_place * rows, rows, 0, NG, 0, NG)
    real_part, imag_part = (real_part * kernel, imag_part * kernel)
    real_part, imag_part = transform_axis(real_part, imag_part, inverse, 1)
    both = lax.all_to_all(jnp.stack([real_part, imag_part]), "slab", 2, 1, tiled=True)
    real_part, imag_part = both[0], both[1]
    real_part, imag_part = transform_axis(real_part, imag_part, inverse, 0)
    hartree = real_output_axis(real_part, imag_part, inverse, 2)
    core_share = lax.dynamic_slice_in_dim(core_density, slab_place * rows, rows, 1)
    outer_share = lax.dynamic_slice_in_dim(external, slab_place * rows, rows, 1)
    share_value = local_terms(share, core_share, outer_share, hartree)
    slab_energy = jnp.sum(share_value * share) / (NG * NG * NG)
    extra = jnp.zeros(share_value.shape[:-1] + (1,), jnp.float32).at[0, 0, 0].set(slab_energy)
    gathered = lax.all_gather(jnp.concatenate([share_value, extra], axis=-1), "slab", axis=1, tiled=True)
    energy = kinetic_total + jnp.sum(gathered[0, ::rows, NG])
    return gathered[..., :NG], energy


def per_device(coeffs, occupation, core_density, external):
    forward, backward = wave_tables()
    kinetic = kinetic_table()
    local_bands = coeffs.shape[0]
    total_bands = local_bands * lax.axis_size("band") * lax.axis_size("slab")
    waves = coeffs.reshape(local_bands, 2, GC, GC, GC)
    real_in = waves[:, 0]
    imag_in = waves[:, 1]
    weights = occupation / (GC * GC * GC * total_bands)
    grid_r, grid_i = to_grid(real_in, imag_in, forward, 1)
    partial_value = jnp.sum(
        weights[:, None, None, None] * (grid_r * grid_r + grid_i * grid_i), axis=0
    )
    kinetic_part = jnp.sum(
        weights * jnp.sum(kinetic * (real_in * real_in + imag_in * imag_in), axis=(1, 2, 3))
    )
    potential, energy = slab_potential(partial_value, kinetic_part, core_density, external)
    new_r, new_i, first_r, first_i = propagate(
        real_in, imag_in, grid_r, grid_i, potential, kinetic, forward, backward, 1
    )
    new_coeffs = jnp.stack([new_r, new_i], axis=1).reshape(local_bands, 2, GC, GC * GC)
    return (new_coeffs, potential, energy)


def solution(mesh):
    return jax.shard_map(
        per_device,
        mesh=mesh,
        in_specs=(P(("band", "slab"), None, None, None), P(("band", "slab")), P(), P()),
        out_specs=(P(("band", "slab"), None, None, None), P(), P()),
        check_vma=False,
    )
```

```python
import math

import jax
import jax.numpy as jnp
from jax import lax
from jax.sharding import PartitionSpec as P

GC = 48
NG = 96


TWO_PI = 2.0 * math.pi
FOUR_PI = 4.0 * math.pi
SCREEN = 0.05
STEP_DT = 0.1
XC_COEF = -((3.0 / math.pi) ** (1.0 / 3.0))


def contract(operand, table, position, precision=lax.Precision.HIGHEST):
    labels = "abcd"[: operand.ndim]
    pattern = (
        labels + ",r" + labels[position] + "->" + labels[:position] + "r" + labels[position + 1 :]
    )
    return jnp.einsum(pattern, operand, table, precision=precision)


def transform_axis(real_in, imag_in, tables, position, precision=lax.Precision.HIGHEST):
    cosine, sine = tables
    real_out = contract(real_in, cosine, position, precision) - contract(imag_in, sine, position, precision)
    imag_out = contract(real_in, sine, position, precision) + contract(imag_in, cosine, position, precision)
    return (real_out, imag_out)


def real_input_axis(values, tables, position):
    return (contract(values, tables[0], position), contract(values, tables[1], position))


def real_output_axis(real_in, imag_in, tables, position):
    return contract(real_in, tables[0], position) - contract(imag_in, tables[1], position)


def phase_table(outer, inner, sign_value, factor):
    product = jnp.mod(outer[:, None] * inner[None, :], NG)
    angles = sign_value * TWO_PI / NG * product.astype(jnp.float32)
    return (jnp.cos(angles) * factor, jnp.sin(angles) * factor)


def frequencies():
    return jnp.arange(GC, dtype=jnp.int32) - GC // 2


def wave_tables():
    points = jnp.arange(NG, dtype=jnp.int32)
    return (
        phase_table(points, frequencies(), 1.0, 1.0),
        phase_table(frequencies(), points, -1.0, 1.0 / NG),
    )


def poisson_tables():
    points = jnp.arange(NG, dtype=jnp.int32)
    return (phase_table(points, points, -1.0, 1.0 / NG), phase_table(points, points, 1.0, 1.0))


def kinetic_table():
    squares = (frequencies().astype(jnp.float32) * (TWO_PI / NG)) ** 2
    return 0.5 * (squares[:, None, None] + squares[None, :, None] + squares[None, None, :])


def folded_squares(start, count):
    index = start + jnp.arange(count, dtype=jnp.int32)
    folded = jnp.where(index < NG // 2, index, index - NG)
    return ((folded.astype(jnp.float32) * (TWO_PI / NG)) ** 2, folded == 0)


def screened_kernel(start_x, count_x, start_y, count_y, start_z, count_z):
    square_x, zero_x = folded_squares(start_x, count_x)
    square_y, zero_y = folded_squares(start_y, count_y)
    square_z, zero_z = folded_squares(start_z, count_z)
    total = square_x[:, None, None] + square_y[None, :, None] + square_z[None, None, :]
    anchor = zero_x[:, None, None] & zero_y[None, :, None] & zero_z[None, None, :]
    return jnp.where(anchor, 0.0, FOUR_PI / (total + SCREEN))


def to_grid(real_in, imag_in, forward, offset, precision=lax.Precision.HIGHEST):
    for position in (offset + 2, offset + 1, offset):
        real_in, imag_in = transform_axis(real_in, imag_in, forward, position, precision)
    return (real_in, imag_in)


def to_coeffs(real_in, imag_in, backward, offset, precision=lax.Precision.HIGHEST):
    for position in (offset, offset + 1, offset + 2):
        real_in, imag_in = transform_axis(real_in, imag_in, backward, position, precision)
    return (real_in, imag_in)


def propagate(real_in, imag_in, grid_r, grid_i, potential, kinetic, forward, backward, offset):
    fast = lax.Precision.HIGH
    back_r, back_i = to_coeffs(potential * grid_r, potential * grid_i, backward, offset, fast)
    first_r = kinetic * real_in + back_r
    first_i = kinetic * imag_in + back_i
    next_r, next_i = to_grid(first_r, first_i, forward, offset, fast)
    back_r, back_i = to_coeffs(potential * next_r, potential * next_i, backward, offset, fast)
    second_r = kinetic * first_r + back_r
    second_i = kinetic * first_i + back_i
    new_r = real_in + STEP_DT * first_i - 0.5 * STEP_DT * STEP_DT * second_r
    new_i = imag_in - STEP_DT * first_r - 0.5 * STEP_DT * STEP_DT * second_i
    return (new_r, new_i, first_r, first_i)


def local_terms(density_part, core_part, external_part, hartree_part):
    return external_part + hartree_part + XC_COEF * jnp.cbrt(density_part + core_part)


def reduce_density(partial_value, kinetic_part):
    band_count = lax.axis_size("band")
    slab_count = lax.axis_size("slab")
    rows_x = NG // band_count
    rows_y = NG // slab_count
    pieces = partial_value.reshape(band_count, rows_x, slab_count, rows_y, NG)
    pieces = pieces.transpose(0, 2, 1, 3, 4).reshape(band_count * slab_count, rows_x, rows_y, NG)
    extra = jnp.zeros(pieces.shape[:-1] + (1,), jnp.float32).at[:, 0, 0, 0].set(kinetic_part)
    pieces = jnp.concatenate([pieces, extra], axis=-1)
    pieces = lax.all_to_all(pieces, ("band", "slab"), 0, 0, tiled=True)
    block = jnp.sum(pieces, axis=0)
    kinetic_total = block[0, 0, NG]
    block = block[..., :NG]
    spread = jnp.broadcast_to(block[None], (band_count,) + block.shape)
    spread = lax.all_to_all(spread, "band", 0, 0, tiled=True)
    return spread.reshape(NG, rows_y, NG), kinetic_total


def slab_potential(partial_value, kinetic_part, core_density, external):
    slab_count = lax.axis_size("slab")
    rows = NG // slab_count
    slab_place = lax.axis_index("slab")
    forward, inverse = poisson_tables()
    share, kinetic_total = reduce_density(partial_value, kinetic_part)
    real_part, imag_part = real_input_axis(share, forward, 2)
    real_part, imag_part = transform_axis(real_part, imag_part, forward, 0)
    real_part, imag_part = (
        lax.all_to_all(real_part, "slab", split_axis=0, concat_axis=1, tiled=True),
        lax.all_to_all(imag_part, "slab", split_axis=0, concat_axis=1, tiled=True),
    )
    real_part, imag_part = transform_axis(real_part, imag_part, forward, 1)
    kernel = screened_kernel(slab_place * rows, rows, 0, NG, 0, NG)
    real_part, imag_part = (real_part * kernel, imag_part * kernel)
    real_part, imag_part = transform_axis(real_part, imag_part, inverse, 1)
    real_part, imag_part = (
        lax.all_to_all(real_part, "slab", split_axis=1, concat_axis=0, tiled=True),
        lax.all_to_all(imag_part, "slab", split_axis=1, concat_axis=0, tiled=True),
    )
    real_part, imag_part = transform_axis(real_part, imag_part, inverse, 0)
    hartree = real_output_axis(real_part, imag_part, inverse, 2)
    core_share = lax.dynamic_slice_in_dim(core_density, slab_place * rows, rows, 1)
    outer_share = lax.dynamic_slice_in_dim(external, slab_place * rows, rows, 1)
    share_value = local_terms(share, core_share, outer_share, hartree)
    slab_energy = jnp.sum(share_value * share) / (NG * NG * NG)
    extra = jnp.zeros(share_value.shape[:-1] + (1,), jnp.float32).at[0, 0, 0].set(slab_energy)
    gathered = lax.all_gather(jnp.concatenate([share_value, extra], axis=-1), "slab", axis=1, tiled=True)
    energy = kinetic_total + jnp.sum(gathered[0, ::rows, NG])
    return gathered[..., :NG], energy


def per_device(coeffs, occupation, core_density, external):
    forward, backward = wave_tables()
    kinetic = kinetic_table()
    local_bands = coeffs.shape[0]
    total_bands = local_bands * lax.axis_size("band") * lax.axis_size("slab")
    waves = coeffs.reshape(local_bands, 2, GC, GC, GC)
    real_in = waves[:, 0]
    imag_in = waves[:, 1]
    weights = occupation / (GC * GC * GC * total_bands)
    grid_r, grid_i = to_grid(real_in, imag_in, forward, 1)
    partial_value = jnp.sum(
        weights[:, None, None, None] * (grid_r * grid_r + grid_i * grid_i), axis=0
    )
    kinetic_part = jnp.sum(
        weights * jnp.sum(kinetic * (real_in * real_in + imag_in * imag_in), axis=(1, 2, 3))
    )
    potential, energy = slab_potential(partial_value, kinetic_part, core_density, external)
    new_r, new_i, first_r, first_i = propagate(
        real_in, imag_in, grid_r, grid_i, potential, kinetic, forward, backward, 1
    )
    new_coeffs = jnp.stack([new_r, new_i], axis=1).reshape(local_bands, 2, GC, GC * GC)
    return (new_coeffs, potential, energy)


def solution(mesh):
    return jax.shard_map(
        per_device,
        mesh=mesh,
        in_specs=(P(("band", "slab"), None, None, None), P(("band", "slab")), P(), P()),
        out_specs=(P(("band", "slab"), None, None, None), P(), P()),
        check_vma=False,
    )
```

```python
import math

import jax
import jax.numpy as jnp
from jax import lax
from jax.sharding import PartitionSpec as P

GC = 48
NG = 96


TWO_PI = 2.0 * math.pi
FOUR_PI = 4.0 * math.pi
SCREEN = 0.05
STEP_DT = 0.1
XC_COEF = -((3.0 / math.pi) ** (1.0 / 3.0))


def contract(operand, table, position, precision=lax.Precision.HIGHEST):
    labels = "abcd"[: operand.ndim]
    pattern = (
        labels + ",r" + labels[position] + "->" + labels[:position] + "r" + labels[position + 1 :]
    )
    return jnp.einsum(pattern, operand, table, precision=precision)


def transform_axis(real_in, imag_in, tables, position, precision=lax.Precision.HIGHEST):
    cosine, sine = tables
    real_out = contract(real_in, cosine, position, precision) - contract(imag_in, sine, position, precision)
    imag_out = contract(real_in, sine, position, precision) + contract(imag_in, cosine, position, precision)
    return (real_out, imag_out)


def real_input_axis(values, tables, position):
    return (contract(values, tables[0], position), contract(values, tables[1], position))


def real_output_axis(real_in, imag_in, tables, position):
    return contract(real_in, tables[0], position) - contract(imag_in, tables[1], position)


def phase_table(outer, inner, sign_value, factor):
    product = jnp.mod(outer[:, None] * inner[None, :], NG)
    angles = sign_value * TWO_PI / NG * product.astype(jnp.float32)
    return (jnp.cos(angles) * factor, jnp.sin(angles) * factor)


def frequencies():
    return jnp.arange(GC, dtype=jnp.int32) - GC // 2


def wave_tables():
    points = jnp.arange(NG, dtype=jnp.int32)
    return (
        phase_table(points, frequencies(), 1.0, 1.0),
        phase_table(frequencies(), points, -1.0, 1.0 / NG),
    )


def poisson_tables():
    points = jnp.arange(NG, dtype=jnp.int32)
    return (phase_table(points, points, -1.0, 1.0 / NG), phase_table(points, points, 1.0, 1.0))


def kinetic_table():
    squares = (frequencies().astype(jnp.float32) * (TWO_PI / NG)) ** 2
    return 0.5 * (squares[:, None, None] + squares[None, :, None] + squares[None, None, :])


def folded_squares(start, count):
    index = start + jnp.arange(count, dtype=jnp.int32)
    folded = jnp.where(index < NG // 2, index, index - NG)
    return ((folded.astype(jnp.float32) * (TWO_PI / NG)) ** 2, folded == 0)


def screened_kernel(start_x, count_x, start_y, count_y, start_z, count_z):
    square_x, zero_x = folded_squares(start_x, count_x)
    square_y, zero_y = folded_squares(start_y, count_y)
    square_z, zero_z = folded_squares(start_z, count_z)
    total = square_x[:, None, None] + square_y[None, :, None] + square_z[None, None, :]
    anchor = zero_x[:, None, None] & zero_y[None, :, None] & zero_z[None, None, :]
    return jnp.where(anchor, 0.0, FOUR_PI / (total + SCREEN))


def to_grid(real_in, imag_in, forward, offset, precision=lax.Precision.HIGHEST):
    for position in (offset + 2, offset + 1, offset):
        real_in, imag_in = transform_axis(real_in, imag_in, forward, position, precision)
    return (real_in, imag_in)


def to_coeffs(real_in, imag_in, backward, offset, precision=lax.Precision.HIGHEST):
    for position in (offset, offset + 1, offset + 2):
        real_in, imag_in = transform_axis(real_in, imag_in, backward, position, precision)
    return (real_in, imag_in)


def propagate(real_in, imag_in, grid_r, grid_i, potential, kinetic, forward, backward, offset):
    fast = lax.Precision.HIGH
    back_r, back_i = to_coeffs(potential * grid_r, potential * grid_i, backward, offset, fast)
    first_r = kinetic * real_in + back_r
    first_i = kinetic * imag_in + back_i
    next_r, next_i = to_grid(first_r, first_i, forward, offset, fast)
    back_r, back_i = to_coeffs(potential * next_r, potential * next_i, backward, offset, fast)
    second_r = kinetic * first_r + back_r
    second_i = kinetic * first_i + back_i
    new_r = real_in + STEP_DT * first_i - 0.5 * STEP_DT * STEP_DT * second_r
    new_i = imag_in - STEP_DT * first_r - 0.5 * STEP_DT * STEP_DT * second_i
    return (new_r, new_i, first_r, first_i)


def local_terms(density_part, core_part, external_part, hartree_part):
    return external_part + hartree_part + XC_COEF * jnp.cbrt(density_part + core_part)


def reduce_density(partial_value, kinetic_part):
    band_count = lax.axis_size("band")
    slab_count = lax.axis_size("slab")
    rows_x = NG // band_count
    rows_y = NG // slab_count
    pieces = partial_value.reshape(band_count, rows_x, slab_count, rows_y, NG)
    pieces = pieces.transpose(0, 2, 1, 3, 4).reshape(band_count * slab_count, rows_x, rows_y, NG)
    extra = jnp.zeros(pieces.shape[:-1] + (1,), jnp.float32).at[:, 0, 0, 0].set(kinetic_part)
    pieces = jnp.concatenate([pieces, extra], axis=-1)
    pieces = lax.all_to_all(pieces, ("band", "slab"), 0, 0, tiled=True)
    block = jnp.sum(pieces, axis=0)
    return block[..., :NG], block[0, 0, NG]


def pencil_potential(partial_value, kinetic_part, core_density, external):
    band_count = lax.axis_size("band")
    slab_count = lax.axis_size("slab")
    rows_x = NG // band_count
    rows_y = NG // slab_count
    band_place = lax.axis_index("band")
    slab_place = lax.axis_index("slab")
    forward, inverse = poisson_tables()
    block, kinetic_total = reduce_density(partial_value, kinetic_part)
    real_part, imag_part = real_input_axis(block, forward, 2)
    both = lax.all_to_all(jnp.stack([real_part, imag_part]), "band", 3, 1, tiled=True)
    real_part, imag_part = transform_axis(both[0], both[1], forward, 0)
    both = lax.all_to_all(jnp.stack([real_part, imag_part]), "slab", 1, 2, tiled=True)
    real_part, imag_part = transform_axis(both[0], both[1], forward, 1)
    kernel = screened_kernel(slab_place * rows_y, rows_y, 0, NG, band_place * rows_x, rows_x)
    real_part, imag_part = (real_part * kernel, imag_part * kernel)
    real_part, imag_part = transform_axis(real_part, imag_part, inverse, 1)
    both = lax.all_to_all(jnp.stack([real_part, imag_part]), "slab", 2, 1, tiled=True)
    real_part, imag_part = transform_axis(both[0], both[1], inverse, 0)
    both = lax.all_to_all(jnp.stack([real_part, imag_part]), "band", 1, 3, tiled=True)
    hartree = real_output_axis(both[0], both[1], inverse, 2)
    core_share = lax.dynamic_slice(core_density, (band_place * rows_x, slab_place * rows_y, 0), block.shape)
    outer_share = lax.dynamic_slice(external, (band_place * rows_x, slab_place * rows_y, 0), block.shape)
    share_value = local_terms(block, core_share, outer_share, hartree)
    pencil_energy = jnp.sum(share_value * block) / (NG * NG * NG)
    extra = jnp.zeros(share_value.shape[:-1] + (1,), jnp.float32).at[0, 0, 0].set(pencil_energy)
    sent = jnp.concatenate([share_value, extra], axis=-1)
    sent = jnp.broadcast_to(sent[None], (band_count * slab_count,) + sent.shape)
    gathered = lax.all_to_all(sent, ("band", "slab"), 0, 0, tiled=True)
    energy = kinetic_total + jnp.sum(gathered[:, 0, 0, NG])
    full = gathered[..., :NG].reshape(band_count, slab_count, rows_x, rows_y, NG)
    full = full.transpose(0, 2, 1, 3, 4).reshape(NG, NG, NG)
    return full, energy


def per_device(coeffs, occupation, core_density, external):
    forward, backward = wave_tables()
    kinetic = kinetic_table()
    local_bands = coeffs.shape[0]
    total_bands = local_bands * lax.axis_size("band") * lax.axis_size("slab")
    waves = coeffs.reshape(local_bands, 2, GC, GC, GC)
    real_in = waves[:, 0]
    imag_in = waves[:, 1]
    weights = occupation / (GC * GC * GC * total_bands)
    grid_r, grid_i = to_grid(real_in, imag_in, forward, 1)
    partial_value = jnp.sum(
        weights[:, None, None, None] * (grid_r * grid_r + grid_i * grid_i), axis=0
    )
    kinetic_part = jnp.sum(
        weights * jnp.sum(kinetic * (real_in * real_in + imag_in * imag_in), axis=(1, 2, 3))
    )
    potential, energy = pencil_potential(partial_value, kinetic_part, core_density, external)
    new_r, new_i, first_r, first_i = propagate(
        real_in, imag_in, grid_r, grid_i, potential, kinetic, forward, backward, 1
    )
    new_coeffs = jnp.stack([new_r, new_i], axis=1).reshape(local_bands, 2, GC, GC * GC)
    return (new_coeffs, potential, energy)


def solution(mesh):
    return jax.shard_map(
        per_device,
        mesh=mesh,
        in_specs=(P(("band", "slab"), None, None, None), P(("band", "slab")), P(), P()),
        out_specs=(P(("band", "slab"), None, None, None), P(), P()),
        check_vma=False,
    )
```

```python
import math

import jax
import jax.numpy as jnp
from jax import lax
from jax.sharding import PartitionSpec as P

GC = 48
NG = 96
LANES = 128


TWO_PI = 2.0 * math.pi
FOUR_PI = 4.0 * math.pi
SCREEN = 0.05
STEP_DT = 0.1
XC_COEF = -((3.0 / math.pi) ** (1.0 / 3.0))


def contract(operand, table, position, precision=lax.Precision.HIGHEST):
    labels = "abcd"[: operand.ndim]
    pattern = (
        labels + ",r" + labels[position] + "->" + labels[:position] + "r" + labels[position + 1 :]
    )
    return jnp.einsum(pattern, operand, table, precision=precision)


def transform_axis(real_in, imag_in, tables, position, precision=lax.Precision.HIGHEST):
    cosine, sine = tables
    real_out = contract(real_in, cosine, position, precision) - contract(imag_in, sine, position, precision)
    imag_out = contract(real_in, sine, position, precision) + contract(imag_in, cosine, position, precision)
    return (real_out, imag_out)


def real_input_axis(values, tables, position):
    return (contract(values, tables[0], position), contract(values, tables[1], position))


def real_output_axis(real_in, imag_in, tables, position):
    return contract(real_in, tables[0], position) - contract(imag_in, tables[1], position)


def phase_table(outer, inner, sign_value, factor):
    product = jnp.mod(outer[:, None] * inner[None, :], NG)
    angles = sign_value * TWO_PI / NG * product.astype(jnp.float32)
    return (jnp.cos(angles) * factor, jnp.sin(angles) * factor)


def frequencies():
    return jnp.arange(GC, dtype=jnp.int32) - GC // 2


def wave_tables():
    points = jnp.arange(NG, dtype=jnp.int32)
    return (
        phase_table(points, frequencies(), 1.0, 1.0),
        phase_table(frequencies(), points, -1.0, 1.0 / NG),
    )


def poisson_tables():
    points = jnp.arange(NG, dtype=jnp.int32)
    return (phase_table(points, points, -1.0, 1.0 / NG), phase_table(points, points, 1.0, 1.0))


def kinetic_table():
    squares = (frequencies().astype(jnp.float32) * (TWO_PI / NG)) ** 2
    return 0.5 * (squares[:, None, None] + squares[None, :, None] + squares[None, None, :])


def folded_squares(start, count):
    index = start + jnp.arange(count, dtype=jnp.int32)
    folded = jnp.where(index < NG // 2, index, index - NG)
    return ((folded.astype(jnp.float32) * (TWO_PI / NG)) ** 2, folded == 0)


def screened_kernel(start_x, count_x, start_y, count_y, start_z, count_z):
    square_x, zero_x = folded_squares(start_x, count_x)
    square_y, zero_y = folded_squares(start_y, count_y)
    square_z, zero_z = folded_squares(start_z, count_z)
    total = square_x[:, None, None] + square_y[None, :, None] + square_z[None, None, :]
    anchor = zero_x[:, None, None] & zero_y[None, :, None] & zero_z[None, None, :]
    return jnp.where(anchor, 0.0, FOUR_PI / (total + SCREEN))


def to_grid(real_in, imag_in, forward, offset, precision=lax.Precision.HIGHEST):
    for position in (offset + 2, offset + 1, offset):
        real_in, imag_in = transform_axis(real_in, imag_in, forward, position, precision)
    return (real_in, imag_in)


def to_coeffs(real_in, imag_in, backward, offset, precision=lax.Precision.HIGHEST):
    for position in (offset, offset + 1, offset + 2):
        real_in, imag_in = transform_axis(real_in, imag_in, backward, position, precision)
    return (real_in, imag_in)


def propagate(real_in, imag_in, grid_r, grid_i, potential, kinetic, forward, backward, offset):
    fast = lax.Precision.HIGH
    back_r, back_i = to_coeffs(potential * grid_r, potential * grid_i, backward, offset, fast)
    first_r = kinetic * real_in + back_r
    first_i = kinetic * imag_in + back_i
    next_r, next_i = to_grid(first_r, first_i, forward, offset, fast)
    back_r, back_i = to_coeffs(potential * next_r, potential * next_i, backward, offset, fast)
    second_r = kinetic * first_r + back_r
    second_i = kinetic * first_i + back_i
    new_r = real_in + STEP_DT * first_i - 0.5 * STEP_DT * STEP_DT * second_r
    new_i = imag_in - STEP_DT * first_r - 0.5 * STEP_DT * STEP_DT * second_i
    return (new_r, new_i, first_r, first_i)


def local_terms(density_part, core_part, external_part, hartree_part):
    return external_part + hartree_part + XC_COEF * jnp.cbrt(density_part + core_part)


def reduce_density(partial_value, kinetic_part):
    band_count = lax.axis_size("band")
    slab_count = lax.axis_size("slab")
    rows_x = NG // band_count
    rows_y = NG // slab_count
    pieces = partial_value.reshape(band_count, rows_x, slab_count, rows_y, NG)
    pieces = pieces.transpose(0, 2, 1, 3, 4).reshape(band_count * slab_count, -1, LANES)
    extra = jnp.zeros((pieces.shape[0], 1, LANES), jnp.float32).at[:, 0, 0].set(kinetic_part)
    pieces = jnp.concatenate([pieces, extra], axis=1)
    pieces = lax.all_to_all(pieces, ("band", "slab"), 0, 0, tiled=True)
    block = jnp.sum(pieces, axis=0)
    return block[:-1].reshape(rows_x, rows_y, NG), block[-1, 0]


def pencil_potential(partial_value, kinetic_part, core_density, external):
    band_count = lax.axis_size("band")
    slab_count = lax.axis_size("slab")
    rows_x = NG // band_count
    rows_y = NG // slab_count
    band_place = lax.axis_index("band")
    slab_place = lax.axis_index("slab")
    forward, inverse = poisson_tables()
    block, kinetic_total = reduce_density(partial_value, kinetic_part)
    real_part, imag_part = real_input_axis(block, forward, 2)
    both = lax.all_to_all(jnp.stack([real_part, imag_part]), "band", 3, 1, tiled=True)
    real_part, imag_part = transform_axis(both[0], both[1], forward, 0)
    both = lax.all_to_all(jnp.stack([real_part, imag_part]), "slab", 1, 2, tiled=True)
    real_part, imag_part = transform_axis(both[0], both[1], forward, 1)
    kernel = screened_kernel(slab_place * rows_y, rows_y, 0, NG, band_place * rows_x, rows_x)
    real_part, imag_part = (real_part * kernel, imag_part * kernel)
    real_part, imag_part = transform_axis(real_part, imag_part, inverse, 1)
    both = lax.all_to_all(jnp.stack([real_part, imag_part]), "slab", 2, 1, tiled=True)
    real_part, imag_part = transform_axis(both[0], both[1], inverse, 0)
    both = lax.all_to_all(jnp.stack([real_part, imag_part]), "band", 1, 3, tiled=True)
    hartree = real_output_axis(both[0], both[1], inverse, 2)
    core_share = lax.dynamic_slice(core_density, (band_place * rows_x, slab_place * rows_y, 0), block.shape)
    outer_share = lax.dynamic_slice(external, (band_place * rows_x, slab_place * rows_y, 0), block.shape)
    share_value = local_terms(block, core_share, outer_share, hartree)
    pencil_energy = jnp.sum(share_value * block) / (NG * NG * NG)
    extra = jnp.zeros((1, LANES), jnp.float32).at[0, 0].set(pencil_energy)
    sent = jnp.concatenate([share_value.reshape(-1, LANES), extra], axis=0)
    sent = jnp.broadcast_to(sent[None], (band_count * slab_count,) + sent.shape)
    gathered = lax.all_to_all(sent, ("band", "slab"), 0, 0, tiled=True)
    energy = kinetic_total + jnp.sum(gathered[:, -1, 0])
    full = gathered[:, :-1].reshape(band_count, slab_count, rows_x, rows_y, NG)
    full = full.transpose(0, 2, 1, 3, 4).reshape(NG, NG, NG)
    return full, energy


def per_device(coeffs, occupation, core_density, external):
    forward, backward = wave_tables()
    kinetic = kinetic_table()
    local_bands = coeffs.shape[0]
    total_bands = local_bands * lax.axis_size("band") * lax.axis_size("slab")
    waves = coeffs.reshape(local_bands, 2, GC, GC, GC)
    real_in = waves[:, 0]
    imag_in = waves[:, 1]
    weights = occupation / (GC * GC * GC * total_bands)
    grid_r, grid_i = to_grid(real_in, imag_in, forward, 1)
    partial_value = jnp.sum(
        weights[:, None, None, None] * (grid_r * grid_r + grid_i * grid_i), axis=0
    )
    kinetic_part = jnp.sum(
        weights * jnp.sum(kinetic * (real_in * real_in + imag_in * imag_in), axis=(1, 2, 3))
    )
    potential, energy = pencil_potential(partial_value, kinetic_part, core_density, external)
    new_r, new_i, first_r, first_i = propagate(
        real_in, imag_in, grid_r, grid_i, potential, kinetic, forward, backward, 1
    )
    new_coeffs = jnp.stack([new_r, new_i], axis=1).reshape(local_bands, 2, GC, GC * GC)
    return (new_coeffs, potential, energy)


def solution(mesh):
    return jax.shard_map(
        per_device,
        mesh=mesh,
        in_specs=(P(("band", "slab"), None, None, None), P(("band", "slab")), P(), P()),
        out_specs=(P(("band", "slab"), None, None, None), P(), P()),
        check_vma=False,
    )
```

```python
import math

import jax
import jax.numpy as jnp
from jax import lax
from jax.sharding import PartitionSpec as P

GC = 48
NG = 96
LANES = 128


TWO_PI = 2.0 * math.pi
FOUR_PI = 4.0 * math.pi
SCREEN = 0.05
STEP_DT = 0.1
XC_COEF = -((3.0 / math.pi) ** (1.0 / 3.0))


def contract(operand, table, position, precision=lax.Precision.HIGHEST):
    labels = "abcd"[: operand.ndim]
    pattern = (
        labels + ",r" + labels[position] + "->" + labels[:position] + "r" + labels[position + 1 :]
    )
    return jnp.einsum(pattern, operand, table, precision=precision)


def transform_axis(real_in, imag_in, tables, position, precision=lax.Precision.HIGHEST):
    cosine, sine = tables
    real_out = contract(real_in, cosine, position, precision) - contract(imag_in, sine, position, precision)
    imag_out = contract(real_in, sine, position, precision) + contract(imag_in, cosine, position, precision)
    return (real_out, imag_out)


def real_input_axis(values, tables, position):
    return (contract(values, tables[0], position), contract(values, tables[1], position))


def real_output_axis(real_in, imag_in, tables, position):
    return contract(real_in, tables[0], position) - contract(imag_in, tables[1], position)


def phase_table(outer, inner, sign_value, factor):
    product = jnp.mod(outer[:, None] * inner[None, :], NG)
    angles = sign_value * TWO_PI / NG * product.astype(jnp.float32)
    return (jnp.cos(angles) * factor, jnp.sin(angles) * factor)


def frequencies():
    return jnp.arange(GC, dtype=jnp.int32) - GC // 2


def wave_tables():
    points = jnp.arange(NG, dtype=jnp.int32)
    return (
        phase_table(points, frequencies(), 1.0, 1.0),
        phase_table(frequencies(), points, -1.0, 1.0 / NG),
    )


def poisson_tables():
    points = jnp.arange(NG, dtype=jnp.int32)
    return (phase_table(points, points, -1.0, 1.0 / NG), phase_table(points, points, 1.0, 1.0))


def kinetic_table():
    squares = (frequencies().astype(jnp.float32) * (TWO_PI / NG)) ** 2
    return 0.5 * (squares[:, None, None] + squares[None, :, None] + squares[None, None, :])


def folded_squares(start, count):
    index = start + jnp.arange(count, dtype=jnp.int32)
    folded = jnp.where(index < NG // 2, index, index - NG)
    return ((folded.astype(jnp.float32) * (TWO_PI / NG)) ** 2, folded == 0)


def screened_kernel(start_x, count_x, start_y, count_y, start_z, count_z):
    square_x, zero_x = folded_squares(start_x, count_x)
    square_y, zero_y = folded_squares(start_y, count_y)
    square_z, zero_z = folded_squares(start_z, count_z)
    total = square_x[:, None, None] + square_y[None, :, None] + square_z[None, None, :]
    anchor = zero_x[:, None, None] & zero_y[None, :, None] & zero_z[None, None, :]
    return jnp.where(anchor, 0.0, FOUR_PI / (total + SCREEN))


def to_grid(real_in, imag_in, forward, offset, precision=lax.Precision.HIGHEST):
    for position in (offset + 2, offset + 1, offset):
        real_in, imag_in = transform_axis(real_in, imag_in, forward, position, precision)
    return (real_in, imag_in)


def to_coeffs(real_in, imag_in, backward, offset, precision=lax.Precision.HIGHEST):
    for position in (offset, offset + 1, offset + 2):
        real_in, imag_in = transform_axis(real_in, imag_in, backward, position, precision)
    return (real_in, imag_in)


def propagate(real_in, imag_in, grid_halves, potential_halves, kinetic, forward, backward, offset):
    fast = lax.Precision.HIGH
    parts_r, parts_i = [], []
    for (grid_r, grid_i), potential in zip(grid_halves, potential_halves):
        part_r, part_i = transform_axis(potential * grid_r, potential * grid_i, backward, offset, fast)
        part_r, part_i = transform_axis(part_r, part_i, backward, offset + 1, fast)
        parts_r.append(part_r)
        parts_i.append(part_i)
    back_r, back_i = transform_axis(
        jnp.concatenate(parts_r, axis=-1), jnp.concatenate(parts_i, axis=-1), backward, offset + 2, fast
    )
    potential = jnp.concatenate(potential_halves, axis=-1)
    first_r = kinetic * real_in + back_r
    first_i = kinetic * imag_in + back_i
    next_r, next_i = to_grid(first_r, first_i, forward, offset, fast)
    back_r, back_i = to_coeffs(potential * next_r, potential * next_i, backward, offset, fast)
    second_r = kinetic * first_r + back_r
    second_i = kinetic * first_i + back_i
    new_r = real_in + STEP_DT * first_i - 0.5 * STEP_DT * STEP_DT * second_r
    new_i = imag_in - STEP_DT * first_r - 0.5 * STEP_DT * STEP_DT * second_i
    return (new_r, new_i, first_r, first_i, potential)


def local_terms(density_part, core_part, external_part, hartree_part):
    return external_part + hartree_part + XC_COEF * jnp.cbrt(density_part + core_part)


def reduce_density(partial_value, kinetic_part):
    band_count = lax.axis_size("band")
    slab_count = lax.axis_size("slab")
    rows_x = NG // band_count
    rows_y = NG // slab_count
    depth = partial_value.shape[-1]
    pieces = partial_value.reshape(band_count, rows_x, slab_count, rows_y, depth)
    pieces = pieces.transpose(0, 2, 1, 3, 4).reshape(band_count * slab_count, -1, LANES)
    extra = jnp.zeros((pieces.shape[0], 1, LANES), jnp.float32).at[:, 0, 0].set(kinetic_part)
    pieces = jnp.concatenate([pieces, extra], axis=1)
    pieces = lax.all_to_all(pieces, ("band", "slab"), 0, 0, tiled=True)
    block = jnp.sum(pieces, axis=0)
    return block[:-1].reshape(rows_x, rows_y, depth), block[-1, 0]


def pencil_potential(partial_halves, kinetic_part, core_density, external):
    band_count = lax.axis_size("band")
    slab_count = lax.axis_size("slab")
    rows_x = NG // band_count
    rows_y = NG // slab_count
    band_place = lax.axis_index("band")
    slab_place = lax.axis_index("slab")
    forward, inverse = poisson_tables()
    block_a, kinetic_total = reduce_density(partial_halves[0], kinetic_part)
    block_b, _ = reduce_density(partial_halves[1], jnp.zeros_like(kinetic_part))
    block = jnp.concatenate([block_a, block_b], axis=-1)
    real_part, imag_part = real_input_axis(block, forward, 2)
    both = lax.all_to_all(jnp.stack([real_part, imag_part]), "band", 3, 1, tiled=True)
    real_part, imag_part = transform_axis(both[0], both[1], forward, 0)
    both = lax.all_to_all(jnp.stack([real_part, imag_part]), "slab", 1, 2, tiled=True)
    real_part, imag_part = transform_axis(both[0], both[1], forward, 1)
    kernel = screened_kernel(slab_place * rows_y, rows_y, 0, NG, band_place * rows_x, rows_x)
    real_part, imag_part = (real_part * kernel, imag_part * kernel)
    real_part, imag_part = transform_axis(real_part, imag_part, inverse, 1)
    both = lax.all_to_all(jnp.stack([real_part, imag_part]), "slab", 2, 1, tiled=True)
    real_part, imag_part = transform_axis(both[0], both[1], inverse, 0)
    both = lax.all_to_all(jnp.stack([real_part, imag_part]), "band", 1, 3, tiled=True)
    hartree = real_output_axis(both[0], both[1], inverse, 2)
    core_share = lax.dynamic_slice(core_density, (band_place * rows_x, slab_place * rows_y, 0), block.shape)
    outer_share = lax.dynamic_slice(external, (band_place * rows_x, slab_place * rows_y, 0), block.shape)
    share_value = local_terms(block, core_share, outer_share, hartree)
    pencil_energy = jnp.sum(share_value * block) / (NG * NG * NG)
    half = NG // 2
    extra = jnp.zeros((1, LANES), jnp.float32).at[0, 0].set(pencil_energy)
    full = []
    for part in range(2):
        sent = share_value[..., part * half:(part + 1) * half].reshape(-1, LANES)
        if part == 0:
            sent = jnp.concatenate([sent, extra], axis=0)
        sent = jnp.broadcast_to(sent[None], (band_count * slab_count,) + sent.shape)
        gathered = lax.all_to_all(sent, ("band", "slab"), 0, 0, tiled=True)
        if part == 0:
            energy = kinetic_total + jnp.sum(gathered[:, -1, 0])
            gathered = gathered[:, :-1]
        piece = gathered.reshape(band_count, slab_count, rows_x, rows_y, half)
        full.append(piece.transpose(0, 2, 1, 3, 4).reshape(NG, NG, half))
    return full, energy


def per_device(coeffs, occupation, core_density, external):
    forward, backward = wave_tables()
    kinetic = kinetic_table()
    local_bands = coeffs.shape[0]
    total_bands = local_bands * lax.axis_size("band") * lax.axis_size("slab")
    waves = coeffs.reshape(local_bands, 2, GC, GC, GC)
    real_in = waves[:, 0]
    imag_in = waves[:, 1]
    weights = occupation / (GC * GC * GC * total_bands)
    half = NG // 2
    wide_r, wide_i = transform_axis(real_in, imag_in, forward, 3)
    grid_halves, partial_halves = [], []
    for part in range(2):
        grid_r = wide_r[..., part * half:(part + 1) * half]
        grid_i = wide_i[..., part * half:(part + 1) * half]
        grid_r, grid_i = transform_axis(grid_r, grid_i, forward, 2)
        grid_r, grid_i = transform_axis(grid_r, grid_i, forward, 1)
        grid_halves.append((grid_r, grid_i))
        partial_halves.append(
            jnp.sum(weights[:, None, None, None] * (grid_r * grid_r + grid_i * grid_i), axis=0)
        )
    kinetic_part = jnp.sum(
        weights * jnp.sum(kinetic * (real_in * real_in + imag_in * imag_in), axis=(1, 2, 3))
    )
    potential_halves, energy = pencil_potential(partial_halves, kinetic_part, core_density, external)
    new_r, new_i, first_r, first_i, potential = propagate(
        real_in, imag_in, grid_halves, potential_halves, kinetic, forward, backward, 1
    )
    new_coeffs = jnp.stack([new_r, new_i], axis=1).reshape(local_bands, 2, GC, GC * GC)
    return (new_coeffs, potential, energy)


def solution(mesh):
    return jax.shard_map(
        per_device,
        mesh=mesh,
        in_specs=(P(("band", "slab"), None, None, None), P(("band", "slab")), P(), P()),
        out_specs=(P(("band", "slab"), None, None, None), P(), P()),
        check_vma=False,
    )
```

```python
import math

import jax
import jax.numpy as jnp
from jax import lax
from jax.sharding import PartitionSpec as P

GC = 48
NG = 96
LANES = 128


TWO_PI = 2.0 * math.pi
FOUR_PI = 4.0 * math.pi
SCREEN = 0.05
STEP_DT = 0.1
XC_COEF = -((3.0 / math.pi) ** (1.0 / 3.0))


def contract(operand, table, position, precision=lax.Precision.HIGHEST):
    labels = "abcd"[: operand.ndim]
    pattern = (
        labels + ",r" + labels[position] + "->" + labels[:position] + "r" + labels[position + 1 :]
    )
    return jnp.einsum(pattern, operand, table, precision=precision)


def transform_axis(real_in, imag_in, tables, position, precision=lax.Precision.HIGHEST):
    cosine, sine = tables
    real_out = contract(real_in, cosine, position, precision) - contract(imag_in, sine, position, precision)
    imag_out = contract(real_in, sine, position, precision) + contract(imag_in, cosine, position, precision)
    return (real_out, imag_out)


def real_input_axis(values, tables, position):
    return (contract(values, tables[0], position), contract(values, tables[1], position))


def real_output_axis(real_in, imag_in, tables, position):
    return contract(real_in, tables[0], position) - contract(imag_in, tables[1], position)


def phase_table(outer, inner, sign_value, factor):
    product = jnp.mod(outer[:, None] * inner[None, :], NG)
    angles = sign_value * TWO_PI / NG * product.astype(jnp.float32)
    return (jnp.cos(angles) * factor, jnp.sin(angles) * factor)


def frequencies():
    return jnp.arange(GC, dtype=jnp.int32) - GC // 2


def wave_tables():
    points = jnp.arange(NG, dtype=jnp.int32)
    return (
        phase_table(points, frequencies(), 1.0, 1.0),
        phase_table(frequencies(), points, -1.0, 1.0 / NG),
    )


def poisson_tables():
    points = jnp.arange(NG, dtype=jnp.int32)
    return (phase_table(points, points, -1.0, 1.0 / NG), phase_table(points, points, 1.0, 1.0))


def kinetic_table():
    squares = (frequencies().astype(jnp.float32) * (TWO_PI / NG)) ** 2
    return 0.5 * (squares[:, None, None] + squares[None, :, None] + squares[None, None, :])


def folded_squares(start, count):
    index = start + jnp.arange(count, dtype=jnp.int32)
    folded = jnp.where(index < NG // 2, index, index - NG)
    return ((folded.astype(jnp.float32) * (TWO_PI / NG)) ** 2, folded == 0)


def screened_kernel(start_x, count_x, start_y, count_y, start_z, count_z):
    square_x, zero_x = folded_squares(start_x, count_x)
    square_y, zero_y = folded_squares(start_y, count_y)
    square_z, zero_z = folded_squares(start_z, count_z)
    total = square_x[:, None, None] + square_y[None, :, None] + square_z[None, None, :]
    anchor = zero_x[:, None, None] & zero_y[None, :, None] & zero_z[None, None, :]
    return jnp.where(anchor, 0.0, FOUR_PI / (total + SCREEN))


def to_grid(real_in, imag_in, forward, offset, precision=lax.Precision.HIGHEST):
    for position in (offset + 2, offset + 1, offset):
        real_in, imag_in = transform_axis(real_in, imag_in, forward, position, precision)
    return (real_in, imag_in)


def to_coeffs(real_in, imag_in, backward, offset, precision=lax.Precision.HIGHEST):
    for position in (offset, offset + 1, offset + 2):
        real_in, imag_in = transform_axis(real_in, imag_in, backward, position, precision)
    return (real_in, imag_in)


def propagate(real_in, imag_in, grid_r, grid_i, potential, kinetic, forward, backward, offset):
    fast = lax.Precision.HIGH
    back_r, back_i = to_coeffs(potential * grid_r, potential * grid_i, backward, offset, fast)
    first_r = kinetic * real_in + back_r
    first_i = kinetic * imag_in + back_i
    next_r, next_i = to_grid(first_r, first_i, forward, offset, fast)
    back_r, back_i = to_coeffs(potential * next_r, potential * next_i, backward, offset, fast)
    second_r = kinetic * first_r + back_r
    second_i = kinetic * first_i + back_i
    new_r = real_in + STEP_DT * first_i - 0.5 * STEP_DT * STEP_DT * second_r
    new_i = imag_in - STEP_DT * first_r - 0.5 * STEP_DT * STEP_DT * second_i
    return (new_r, new_i, first_r, first_i)


def local_terms(density_part, core_part, external_part, hartree_part):
    return external_part + hartree_part + XC_COEF * jnp.cbrt(density_part + core_part)


def reduce_density(partial_value):
    band_count = lax.axis_size("band")
    slab_count = lax.axis_size("slab")
    rows_x = NG // band_count
    rows_y = NG // slab_count
    pieces = partial_value.reshape(band_count, rows_x, slab_count, rows_y, NG)
    pieces = pieces.transpose(0, 2, 1, 3, 4).reshape(band_count * slab_count, -1, LANES)
    pieces = lax.all_to_all(pieces, ("band", "slab"), 0, 0, tiled=True)
    return jnp.sum(pieces, axis=0).reshape(rows_x, rows_y, NG)


def pencil_potential(partial_value, kinetic_part, core_density, external):
    band_count = lax.axis_size("band")
    slab_count = lax.axis_size("slab")
    rows_x = NG // band_count
    rows_y = NG // slab_count
    band_place = lax.axis_index("band")
    slab_place = lax.axis_index("slab")
    forward, inverse = poisson_tables()
    block = reduce_density(partial_value)
    real_part, imag_part = real_input_axis(block, forward, 2)
    both = lax.all_to_all(jnp.stack([real_part, imag_part]), "band", 3, 1, tiled=True)
    real_part, imag_part = transform_axis(both[0], both[1], forward, 0)
    both = lax.all_to_all(jnp.stack([real_part, imag_part]), "slab", 1, 2, tiled=True)
    real_part, imag_part = transform_axis(both[0], both[1], forward, 1)
    kernel = screened_kernel(slab_place * rows_y, rows_y, 0, NG, band_place * rows_x, rows_x)
    real_part, imag_part = (real_part * kernel, imag_part * kernel)
    real_part, imag_part = transform_axis(real_part, imag_part, inverse, 1)
    both = lax.all_to_all(jnp.stack([real_part, imag_part]), "slab", 2, 1, tiled=True)
    real_part, imag_part = transform_axis(both[0], both[1], inverse, 0)
    both = lax.all_to_all(jnp.stack([real_part, imag_part]), "band", 1, 3, tiled=True)
    hartree = real_output_axis(both[0], both[1], inverse, 2)
    core_share = lax.dynamic_slice(core_density, (band_place * rows_x, slab_place * rows_y, 0), block.shape)
    outer_share = lax.dynamic_slice(external, (band_place * rows_x, slab_place * rows_y, 0), block.shape)
    share_value = local_terms(block, core_share, outer_share, hartree)
    pencil_energy = jnp.sum(share_value * block) / (NG * NG * NG)
    extra = jnp.zeros((1, LANES), jnp.float32).at[0, 0].set(kinetic_part + pencil_energy)
    sent = jnp.concatenate([share_value.reshape(-1, LANES), extra], axis=0)
    sent = jnp.broadcast_to(sent[None], (band_count * slab_count,) + sent.shape)
    gathered = lax.all_to_all(sent, ("band", "slab"), 0, 0, tiled=True)
    energy = jnp.sum(gathered[:, -1, 0])
    full = gathered[:, :-1].reshape(band_count, slab_count, rows_x, rows_y, NG)
    full = full.transpose(0, 2, 1, 3, 4).reshape(NG, NG, NG)
    return full, energy


def per_device(coeffs, occupation, core_density, external):
    forward, backward = wave_tables()
    kinetic = kinetic_table()
    local_bands = coeffs.shape[0]
    total_bands = local_bands * lax.axis_size("band") * lax.axis_size("slab")
    waves = coeffs.reshape(local_bands, 2, GC, GC, GC)
    real_in = waves[:, 0]
    imag_in = waves[:, 1]
    weights = occupation / (GC * GC * GC * total_bands)
    grid_r, grid_i = to_grid(real_in, imag_in, forward, 1)
    partial_value = jnp.sum(
        weights[:, None, None, None] * (grid_r * grid_r + grid_i * grid_i), axis=0
    )
    kinetic_part = jnp.sum(
        weights * jnp.sum(kinetic * (real_in * real_in + imag_in * imag_in), axis=(1, 2, 3))
    )
    potential, energy = pencil_potential(partial_value, kinetic_part, core_density, external)
    new_r, new_i, first_r, first_i = propagate(
        real_in, imag_in, grid_r, grid_i, potential, kinetic, forward, backward, 1
    )
    new_coeffs = jnp.stack([new_r, new_i], axis=1).reshape(local_bands, 2, GC, GC * GC)
    return (new_coeffs, potential, energy)


def solution(mesh):
    return jax.shard_map(
        per_device,
        mesh=mesh,
        in_specs=(P(("band", "slab"), None, None, None), P(("band", "slab")), P(), P()),
        out_specs=(P(("band", "slab"), None, None, None), P(), P()),
        check_vma=False,
    )
```

```python
import math

import jax
import jax.numpy as jnp
from jax import lax
from jax.sharding import PartitionSpec as P

GC = 48
NG = 96
LANES = 128


TWO_PI = 2.0 * math.pi
FOUR_PI = 4.0 * math.pi
SCREEN = 0.05
STEP_DT = 0.1
XC_COEF = -((3.0 / math.pi) ** (1.0 / 3.0))


def contract(operand, table, position, precision=lax.Precision.HIGHEST):
    labels = "abcd"[: operand.ndim]
    pattern = (
        labels + ",r" + labels[position] + "->" + labels[:position] + "r" + labels[position + 1 :]
    )
    return jnp.einsum(pattern, operand, table, precision=precision)


def transform_axis(real_in, imag_in, tables, position, precision=lax.Precision.HIGHEST):
    cosine, sine = tables
    real_out = contract(real_in, cosine, position, precision) - contract(imag_in, sine, position, precision)
    imag_out = contract(real_in, sine, position, precision) + contract(imag_in, cosine, position, precision)
    return (real_out, imag_out)


def real_input_axis(values, tables, position):
    return (contract(values, tables[0], position), contract(values, tables[1], position))


def real_output_axis(real_in, imag_in, tables, position):
    return contract(real_in, tables[0], position) - contract(imag_in, tables[1], position)


def phase_table(outer, inner, sign_value, factor):
    product = jnp.mod(outer[:, None] * inner[None, :], NG)
    angles = sign_value * TWO_PI / NG * product.astype(jnp.float32)
    return (jnp.cos(angles) * factor, jnp.sin(angles) * factor)


def frequencies():
    return jnp.arange(GC, dtype=jnp.int32) - GC // 2


def wave_tables():
    points = jnp.arange(NG, dtype=jnp.int32)
    return (
        phase_table(points, frequencies(), 1.0, 1.0),
        phase_table(frequencies(), points, -1.0, 1.0 / NG),
    )


def poisson_tables():
    points = jnp.arange(NG, dtype=jnp.int32)
    return (phase_table(points, points, -1.0, 1.0 / NG), phase_table(points, points, 1.0, 1.0))


def kinetic_table():
    squares = (frequencies().astype(jnp.float32) * (TWO_PI / NG)) ** 2
    return 0.5 * (squares[:, None, None] + squares[None, :, None] + squares[None, None, :])


def folded_squares(start, count):
    index = start + jnp.arange(count, dtype=jnp.int32)
    folded = jnp.where(index < NG // 2, index, index - NG)
    return ((folded.astype(jnp.float32) * (TWO_PI / NG)) ** 2, folded == 0)


def screened_kernel(start_x, count_x, start_y, count_y, start_z, count_z):
    square_x, zero_x = folded_squares(start_x, count_x)
    square_y, zero_y = folded_squares(start_y, count_y)
    square_z, zero_z = folded_squares(start_z, count_z)
    total = square_x[:, None, None] + square_y[None, :, None] + square_z[None, None, :]
    anchor = zero_x[:, None, None] & zero_y[None, :, None] & zero_z[None, None, :]
    return jnp.where(anchor, 0.0, FOUR_PI / (total + SCREEN))


def to_grid(real_in, imag_in, forward, offset, precision=lax.Precision.HIGHEST):
    for position in (offset + 2, offset + 1, offset):
        real_in, imag_in = transform_axis(real_in, imag_in, forward, position, precision)
    return (real_in, imag_in)


def to_coeffs(real_in, imag_in, backward, offset, precision=lax.Precision.HIGHEST):
    for position in (offset, offset + 1, offset + 2):
        real_in, imag_in = transform_axis(real_in, imag_in, backward, position, precision)
    return (real_in, imag_in)


def propagate(real_in, imag_in, grid_r, grid_i, potential, kinetic, forward, backward, offset):
    fast = lax.Precision.HIGH
    back_r, back_i = to_coeffs(potential * grid_r, potential * grid_i, backward, offset, fast)
    first_r = kinetic * real_in + back_r
    first_i = kinetic * imag_in + back_i
    next_r, next_i = to_grid(first_r, first_i, forward, offset, fast)
    back_r, back_i = to_coeffs(potential * next_r, potential * next_i, backward, offset, fast)
    second_r = kinetic * first_r + back_r
    second_i = kinetic * first_i + back_i
    new_r = real_in + STEP_DT * first_i - 0.5 * STEP_DT * STEP_DT * second_r
    new_i = imag_in - STEP_DT * first_r - 0.5 * STEP_DT * STEP_DT * second_i
    return (new_r, new_i, first_r, first_i)


def local_terms(density_part, core_part, external_part, hartree_part):
    return external_part + hartree_part + XC_COEF * jnp.cbrt(density_part + core_part)


def reduce_density(partial_value):
    band_count = lax.axis_size("band")
    slab_count = lax.axis_size("slab")
    rows_x = NG // band_count
    rows_y = NG // slab_count
    pieces = partial_value.reshape(band_count, rows_x, slab_count, rows_y, NG)
    pieces = pieces.transpose(0, 2, 1, 3, 4).reshape(band_count * slab_count, -1, LANES)
    pieces = lax.all_to_all(pieces, ("band", "slab"), 0, 0, tiled=True)
    return jnp.sum(pieces, axis=0).reshape(rows_x, rows_y, NG)


def pencil_potential(partial_value, kinetic_part, core_density, external):
    band_count = lax.axis_size("band")
    slab_count = lax.axis_size("slab")
    rows_x = NG // band_count
    rows_y = NG // slab_count
    band_place = lax.axis_index("band")
    slab_place = lax.axis_index("slab")
    forward, inverse = poisson_tables()
    block = reduce_density(partial_value)
    real_part, imag_part = real_input_axis(block, forward, 2)
    both = lax.all_to_all(jnp.stack([real_part, imag_part]), "band", 3, 1, tiled=True)
    real_part, imag_part = transform_axis(both[0], both[1], forward, 0)
    both = jnp.stack([real_part, imag_part])
    both = jnp.broadcast_to(both[None], (slab_count,) + both.shape)
    both = lax.all_to_all(both, "slab", 0, 0, tiled=True)
    both = jnp.moveaxis(both, 0, 2).reshape(2, NG, NG, rows_x)
    real_part, imag_part = transform_axis(both[0], both[1], forward, 1)
    kernel = screened_kernel(0, NG, 0, NG, band_place * rows_x, rows_x)
    real_part, imag_part = (real_part * kernel, imag_part * kernel)
    own_rows = tuple(lax.dynamic_slice_in_dim(table, slab_place * rows_y, rows_y, 0) for table in inverse)
    real_part, imag_part = transform_axis(real_part, imag_part, own_rows, 1)
    real_part, imag_part = transform_axis(real_part, imag_part, inverse, 0)
    both = lax.all_to_all(jnp.stack([real_part, imag_part]), "band", 1, 3, tiled=True)
    hartree = real_output_axis(both[0], both[1], inverse, 2)
    core_share = lax.dynamic_slice(core_density, (band_place * rows_x, slab_place * rows_y, 0), block.shape)
    outer_share = lax.dynamic_slice(external, (band_place * rows_x, slab_place * rows_y, 0), block.shape)
    share_value = local_terms(block, core_share, outer_share, hartree)
    pencil_energy = jnp.sum(share_value * block) / (NG * NG * NG)
    extra = jnp.zeros((1, LANES), jnp.float32).at[0, 0].set(kinetic_part + pencil_energy)
    sent = jnp.concatenate([share_value.reshape(-1, LANES), extra], axis=0)
    sent = jnp.broadcast_to(sent[None], (band_count * slab_count,) + sent.shape)
    gathered = lax.all_to_all(sent, ("band", "slab"), 0, 0, tiled=True)
    energy = jnp.sum(gathered[:, -1, 0])
    full = gathered[:, :-1].reshape(band_count, slab_count, rows_x, rows_y, NG)
    full = full.transpose(0, 2, 1, 3, 4).reshape(NG, NG, NG)
    return full, energy


def per_device(coeffs, occupation, core_density, external):
    forward, backward = wave_tables()
    kinetic = kinetic_table()
    local_bands = coeffs.shape[0]
    total_bands = local_bands * lax.axis_size("band") * lax.axis_size("slab")
    waves = coeffs.reshape(local_bands, 2, GC, GC, GC)
    real_in = waves[:, 0]
    imag_in = waves[:, 1]
    weights = occupation / (GC * GC * GC * total_bands)
    grid_r, grid_i = to_grid(real_in, imag_in, forward, 1)
    partial_value = jnp.sum(
        weights[:, None, None, None] * (grid_r * grid_r + grid_i * grid_i), axis=0
    )
    kinetic_part = jnp.sum(
        weights * jnp.sum(kinetic * (real_in * real_in + imag_in * imag_in), axis=(1, 2, 3))
    )
    potential, energy = pencil_potential(partial_value, kinetic_part, core_density, external)
    new_r, new_i, first_r, first_i = propagate(
        real_in, imag_in, grid_r, grid_i, potential, kinetic, forward, backward, 1
    )
    new_coeffs = jnp.stack([new_r, new_i], axis=1).reshape(local_bands, 2, GC, GC * GC)
    return (new_coeffs, potential, energy)


def solution(mesh):
    return jax.shard_map(
        per_device,
        mesh=mesh,
        in_specs=(P(("band", "slab"), None, None, None), P(("band", "slab")), P(), P()),
        out_specs=(P(("band", "slab"), None, None, None), P(), P()),
        check_vma=False,
    )
```
